512 devices in a mesh: pipe: 8 (over y, x_lo), expert: 64 (over x_hi, z, core).
Axes of the slice: x: 4 (x_hi: 2, x_lo: 2; x = x_hi * 2 + x_lo), y: 4, z: 16, core: 2. Of those that a mesh axis runs over, the one named last changes fastest.
Arguments:
- fwd_tokens: bfloat16 [8, 1024, 3584], P('pipe', 'expert'), may hold values from -6 to 6
- fwd_routes: int32 [8, 1024, 2], P('pipe', 'expert'), may hold values from 0 to 7, all different within a row; in each aligned block of 16 rows (0 to 15, 16 to 31, ..., all dimensions but the last counted through in order) at most 6 rows name the same one
- fwd_scores: float32 [8, 1024, 2], P('pipe', 'expert'), may hold values from 0.1 to 1
- bwd_tokens: bfloat16 [8, 1024, 3584], P('pipe', 'expert'), may hold values from -6 to 6
- bwd_routes: int32 [8, 1024, 2], P('pipe', 'expert'), may hold values from 0 to 7, all different within a row; in each aligned block of 16 rows (0 to 15, 16 to 31, ..., all dimensions but the last counted through in order) at most 6 rows name the same one
- bwd_scores: float32 [8, 1024, 2], P('pipe', 'expert'), may hold values from 0.1 to 1
- out_grad: bfloat16 [8, 1024, 3584], P('pipe', 'expert'), may hold values from -6 to 6
- gate_weight: bfloat16 [8, 3584, 8192], P('pipe', None, 'expert'), may hold values from -0.09375 to 0.09375
- up_weight: bfloat16 [8, 3584, 8192], P('pipe', None, 'expert'), may hold values from -0.09375 to 0.09375
- down_weight: bfloat16 [8, 8192, 3584], P('pipe', 'expert'), may hold values from -0.1875 to 0.1875
Outputs:
- next_input: bfloat16 [8, 1024, 3584], P('pipe', 'expert')
- prev_grad: bfloat16 [8, 1024, 3584], P('pipe', 'expert')
The draws below stay inside these ranges and needn't reach their ends.
Inputs may be any that keep to these rules, and one draw needn't show every extreme that they name: `fwd_routes`: each row names 2 different experts. Among the 16 rows of one device in one section, no expert is named more than 6 times, a bound that some block reaches. `bwd_routes`: each row names 2 different experts. Among the 16 rows of one device in one section, no expert is named more than 6 times, a bound that some block reaches.
All inputs are finite; a program needn't handle non-finite values.
Results may differ from the reference program's by a relative error of at most 0.011.
Values may be sent and summed in bfloat16 or wider, within the bound.
No kernel may reach another device: no remote copies, remote signals or barrier semaphores. Data moves between devices by JAX's collectives and lax.ppermute only.
A program may use at most 128 MiB of HBM per device.

```python
import math
import jax
import jax.numpy as jnp
import numpy as np

D = 3584
HIDDEN_SIZE = 1024
GROUP = 8
TOPK = 2
TOK_DEV = 16
H_DEV = 128
EXPERTS = 8
SECTIONS = 8
TOKENS = 1024
CAP = 6
N_EXPERT = 64


def steps_of(key, shape, split, least, high):
    gain, own = 1.0, jax.random.fold_in(key, 6)
    for dim, blocks in split:
        draws = jnp.exp(jax.random.uniform(jax.random.fold_in(own, dim), (blocks,), jnp.float32, least / len(split), high / len(split)))
        gain = gain * jnp.repeat(draws, shape[dim] // blocks).reshape([-1 if axis == dim else 1 for axis in range(len(shape))])
    return gain


def shared_out(own_key, own, number, rows, number_of, top, most, lean):
    sequence = jax.random.permutation(own_key, number_of)
    packed, common = load_shares(number_of, rows * top, most, lean, True), load_shares(number_of, rows * top, most, lean, False)
    places = jnp.arange(number_of)

    def named(sizes, rotation):
        used = int((sizes > 0).sum())
        fixed = max(1, used // 4)
        passed = fixed + (places - fixed + rotation * (used - fixed)) % max(1, number_of - fixed)
        return jnp.zeros((number_of,), jnp.int32).at[sequence[jnp.where(places < fixed, places, passed)]].set(jnp.asarray(sizes, jnp.int32))

    sizes = jnp.where(number % 4 == 0, named(packed, number // 4), named(common, number - number // 4 - 1))
    mixed = jax.random.permutation(jax.random.fold_in(own, 3), number_of)
    source_of, taker = mixed[0:number_of // 2 * 2:2], mixed[1:number_of // 2 * 2:2]
    margin = jnp.minimum(sizes[source_of] - 1, most - sizes[taker]) // 2
    margin = jnp.where((source_of == sequence[0]) | (taker == sequence[0]) | (sizes[taker] == 0), 0, jnp.maximum(margin, 0))
    passed = jax.random.randint(jax.random.fold_in(own, 4), (number_of // 2,), 0, 1 << 20) % (margin + 1)
    sizes = sizes.at[source_of].add(-passed).at[taker].add(passed)
    items = jnp.searchsorted(jnp.cumsum(sizes), jnp.arange(rows * top), side="right").astype(jnp.int32)
    grid = items.reshape(top, rows).T
    grid = grid[jax.random.permutation(jax.random.fold_in(own, 1), rows)]
    rotation = jax.random.randint(jax.random.fold_in(own, 2), (rows, 1), 0, top)
    return jnp.take_along_axis(grid, (jnp.arange(top)[None, :] + rotation) % top, axis=1)


def load_shares(count, total, limit, lean, full):
    loads = [(1 << 20) // math.isqrt(rank ** lean) + 1 for rank in range(1, count + 1)]
    largest = limit if full else min(limit, max(-(-total // count), total * loads[0] // sum(loads)))
    least = 1 if total - largest >= count - 1 else 0
    given, spare = [largest] + [least] * (count - 1), total - largest - least * (count - 1)
    while spare > 0:
        candidates = [i for i in range(1, count) if given[i] < largest] or [i for i in range(1, count) if given[i] < limit]
        whole, remaining = sum([loads[i] for i in candidates]), spare
        for i in candidates:
            more = min(limit - given[i], max(1, remaining * loads[i] // whole), spare)
            given[i] = given[i] + more
            spare = spare - more
    return np.array(given)


def noise(stream_key, shape, scale, reach, split=(), kind=jnp.bfloat16):
    result = scale * jax.random.normal(stream_key, shape, jnp.float32)
    if split:
        result = result * steps_of(stream_key, shape, split, -0.22, 0.18)
    return jnp.clip(result, -reach, reach).astype(kind)


def setup_inputs(seed: int = 0) -> dict:
    key_list = jax.random.split(jax.random.key(seed), 11)
    fwd_tokens = noise(key_list[0], (SECTIONS, TOKENS, D), 1.0, 6.0, ((0, 8), (1, 64)))
    fwd_routes_keys = jax.random.split(jax.random.fold_in(key_list[1], 1), SECTIONS * TOKENS // TOK_DEV)
    fwd_routes_turns = jax.random.permutation(jax.random.fold_in(key_list[1], 3), SECTIONS * TOKENS // TOK_DEV)
    fwd_routes = jax.vmap(lambda own, number: shared_out(jax.random.fold_in(key_list[1], 2), own, number, TOK_DEV, EXPERTS, TOPK, CAP, 2))(fwd_routes_keys, fwd_routes_turns).reshape((SECTIONS, TOKENS, TOPK))
    fwd_scores = jnp.clip(jnp.exp(math.log(1.0) - 2.3025851 * jax.random.uniform(key_list[2], (SECTIONS, TOKENS, TOPK), jnp.float32) ** steps_of(key_list[2], (SECTIONS, TOKENS, TOPK), ((0, 8), (1, 64)), -0.2, 0.2)), 0.1, 1.0)
    bwd_tokens = noise(key_list[3], (SECTIONS, TOKENS, D), 1.0, 6.0, ((0, 8), (1, 64)))
    bwd_routes_keys = jax.random.split(jax.random.fold_in(key_list[4], 1), SECTIONS * TOKENS // TOK_DEV)
    bwd_routes_turns = jax.random.permutation(jax.random.fold_in(key_list[4], 3), SECTIONS * TOKENS // TOK_DEV)
    bwd_routes = jax.vmap(lambda own, number: shared_out(jax.random.fold_in(key_list[4], 2), own, number, TOK_DEV, EXPERTS, TOPK, CAP, 2))(bwd_routes_keys, bwd_routes_turns).reshape((SECTIONS, TOKENS, TOPK))
    bwd_scores = jnp.clip(jnp.exp(math.log(1.0) - 2.3025851 * jax.random.uniform(key_list[5], (SECTIONS, TOKENS, TOPK), jnp.float32) ** steps_of(key_list[5], (SECTIONS, TOKENS, TOPK), ((0, 8), (1, 64)), -0.2, 0.2)), 0.1, 1.0)
    out_grad = noise(key_list[6], (SECTIONS, TOKENS, D), 1.0, 6.0, ((0, 8), (1, 64)))
    gate_weight = noise(key_list[7], (SECTIONS, D, EXPERTS * HIDDEN_SIZE), D ** -0.5, 0.09375, ((0, 8), (2, 64)))
    up_weight = noise(key_list[8], (SECTIONS, D, EXPERTS * HIDDEN_SIZE), D ** -0.5, 0.09375, ((0, 8), (2, 64)))
    down_weight = noise(key_list[9], (SECTIONS, EXPERTS * HIDDEN_SIZE, D), HIDDEN_SIZE ** -0.5, 0.1875, ((0, 8), (1, 64)))
    return dict(fwd_tokens=fwd_tokens, fwd_routes=fwd_routes, fwd_scores=fwd_scores, bwd_tokens=bwd_tokens, bwd_routes=bwd_routes, bwd_scores=bwd_scores, out_grad=out_grad, gate_weight=gate_weight, up_weight=up_weight, down_weight=down_weight)


def slot_places(routes):
    blocks = routes.reshape(N_EXPERT, TOK_DEV * TOPK)
    onehot = (blocks[:, :, None] == jnp.arange(EXPERTS, dtype=jnp.int32)[None, None, :]).astype(jnp.int32)
    rank = jnp.cumsum(onehot, axis=1) - onehot
    within = jnp.sum(rank * onehot, axis=2)
    anchor = (jnp.arange(N_EXPERT, dtype=jnp.int32) * CAP)[:, None]
    return blocks.reshape(-1), (anchor + within).reshape(-1).astype(jnp.int32)


def populate_slots(rows, experts_of, places):
    width = rows.shape[-1]
    empty = jnp.zeros((EXPERTS, N_EXPERT * CAP, width), rows.dtype)
    return empty.at[experts_of, places].set(rows)


def section_pass(xf, rf, sf, xb, rb, sb, grad, wg_all, wu_all, wd_all):
    norm_f = sf / jnp.sum(sf, axis=1, keepdims=True)
    norm_b = sb / jnp.sum(sb, axis=1, keepdims=True)
    ef, pf = slot_places(rf)
    expert_batch, param_bundle = slot_places(rb)
    fbuf = populate_slots(jnp.repeat(xf, TOPK, axis=0), ef, pf)
    bbuf = populate_slots(jnp.repeat(xb, TOPK, axis=0), expert_batch, param_bundle)
    queued_rows = (norm_b.reshape(-1)[:, None] * jnp.repeat(grad, TOPK, axis=0).astype(jnp.float32)).astype(jnp.bfloat16)
    gradient_buffer = populate_slots(queued_rows, expert_batch, param_bundle)
    outs = []
    grads = []
    for expert_unit in range(EXPERTS):
        wg = wg_all[:, expert_unit * HIDDEN_SIZE:(expert_unit + 1) * HIDDEN_SIZE]
        wu = wu_all[:, expert_unit * HIDDEN_SIZE:(expert_unit + 1) * HIDDEN_SIZE]
        down_matrix = wd_all[expert_unit * HIDDEN_SIZE:(expert_unit + 1) * HIDDEN_SIZE, :]
        a = jnp.dot(fbuf[expert_unit], wg, preferred_element_type=jnp.float32)
        b = jnp.dot(fbuf[expert_unit], wu, preferred_element_type=jnp.float32)
        h = (jax.nn.silu(a) * b).astype(jnp.bfloat16)
        hs = h.reshape(-1, GROUP, H_DEV).astype(jnp.float32)
        ws = down_matrix.reshape(GROUP, H_DEV, D).astype(jnp.float32)
        parts = jnp.einsum("rgh,ghd->rgd", hs, ws).astype(jnp.bfloat16)
        outs.append(jnp.sum(parts.astype(jnp.float32), axis=1))
        a2 = jnp.dot(bbuf[expert_unit], wg, preferred_element_type=jnp.float32)
        b2 = jnp.dot(bbuf[expert_unit], wu, preferred_element_type=jnp.float32)
        hidden_grad = jnp.einsum("ou,cu->oc", gradient_buffer[expert_unit].astype(jnp.float32), down_matrix.astype(jnp.float32))
        sg = 1.0 / (1.0 + jnp.exp(-a2))
        da = (hidden_grad * b2 * sg * (1.0 + a2 * (1.0 - sg))).astype(jnp.bfloat16)
        db = (hidden_grad * a2 * sg).astype(jnp.bfloat16)
        das = da.reshape(-1, GROUP, H_DEV).astype(jnp.float32)
        dbs = db.reshape(-1, GROUP, H_DEV).astype(jnp.float32)
        wgs = wg.reshape(D, GROUP, H_DEV).astype(jnp.float32)
        wus = wu.reshape(D, GROUP, H_DEV).astype(jnp.float32)
        back = (jnp.einsum("rgh,dgh->rgd", das, wgs) + jnp.einsum("rgh,dgh->rgd", dbs, wus)).astype(jnp.bfloat16)
        grads.append(jnp.sum(back.astype(jnp.float32), axis=1))
    outs = jnp.stack(outs)
    grads = jnp.stack(grads)
    picked = outs[ef, pf].reshape(TOKENS, TOPK, D)
    y = jnp.sum(norm_f[:, :, None] * picked, axis=1).astype(jnp.bfloat16)
    picked_g = grads[expert_batch, param_bundle].reshape(TOKENS, TOPK, D)
    dx = jnp.sum(picked_g, axis=1).astype(jnp.bfloat16)
    return y, dx


def reference(fwd_tokens, fwd_routes, fwd_scores, bwd_tokens, bwd_routes, bwd_scores, out_grad, gate_weight, up_weight, down_weight):
    ys = []
    dxs = []
    for section in range(SECTIONS):
        y, dx = section_pass(fwd_tokens[section], fwd_routes[section], fwd_scores[section],
                             bwd_tokens[section], bwd_routes[section], bwd_scores[section],
                             out_grad[section], gate_weight[section], up_weight[section], down_weight[section])
        ys.append(y)
        dxs.append(dx)
    ys = jnp.stack(ys)
    dxs = jnp.stack(dxs)
    return jnp.roll(ys, 1, axis=0), jnp.roll(dxs, -1, axis=0)
```

```python
import jax
import jax.numpy as jnp
from jax import lax
from jax.sharding import Mesh
from jax.sharding import PartitionSpec as P

GROUP = 8


def from_behind(value, axis, steps):
    count = lax.axis_size(axis)
    pairs = [(source, (source + steps) % count) for source in range(count)]
    return lax.ppermute(value, axis, pairs)


def route_tables(routes, scores, capacity, experts):
    tokens, topk = routes.shape
    flat = routes.reshape(-1)
    onehot = (flat[:, None] == jnp.arange(experts, dtype=jnp.int32)[None, :]).astype(jnp.int32)
    rank = jnp.cumsum(onehot, axis=0) - onehot
    within = jnp.sum(rank * onehot, axis=1)
    slot_ids = (flat * capacity + within).reshape(tokens, topk)
    places = jnp.arange(experts * capacity, dtype=jnp.int32)
    hits = (slot_ids[:, :, None] == places[None, None, :]).astype(jnp.float32)
    normed = scores / jnp.sum(scores, axis=1, keepdims=True)
    member = jnp.sum(hits, axis=1)
    weighted = jnp.sum(hits * normed[:, :, None], axis=1)
    return (member, weighted)


def pick_rows(member, rows):
    slots = jnp.einsum(
        "te,td->ed", member.astype(jnp.bfloat16), rows, preferred_element_type=jnp.float32
    )
    return slots.astype(jnp.bfloat16)


def expert_forward(flat, w_gate, w_up, w_down):
    first = jnp.dot(flat, w_gate, preferred_element_type=jnp.float32)
    second = jnp.dot(flat, w_up, preferred_element_type=jnp.float32)
    hidden = (jax.nn.silu(first) * second).astype(jnp.bfloat16)
    return jnp.dot(hidden, w_down, preferred_element_type=jnp.float32).astype(jnp.bfloat16)


def expert_backward(flat, grads, w_gate, w_up, w_down):
    first = jnp.dot(flat, w_gate, preferred_element_type=jnp.float32)
    second = jnp.dot(flat, w_up, preferred_element_type=jnp.float32)
    d_hidden = lax.dot_general(
        grads, w_down, (((1,), (1,)), ((), ())), preferred_element_type=jnp.float32
    )
    sigm = 1.0 / (1.0 + jnp.exp(-first))
    d_first = (d_hidden * second * sigm * (1.0 + first * (1.0 - sigm))).astype(jnp.bfloat16)
    d_second = (d_hidden * first * sigm).astype(jnp.bfloat16)
    back = lax.dot_general(
        d_first, w_gate, (((1,), (1,)), ((), ())), preferred_element_type=jnp.float32
    )
    back = back + lax.dot_general(
        d_second, w_up, (((1,), (1,)), ((), ())), preferred_element_type=jnp.float32
    )
    return back.astype(jnp.bfloat16)


def body(
    fwd_tokens,
    fwd_routes,
    fwd_scores,
    bwd_tokens,
    bwd_routes,
    bwd_scores,
    out_grad,
    gate_weight,
    up_weight,
    down_weight,
):
    experts = lax.axis_size("eg")
    tokens = fwd_tokens.shape[1]
    topk = fwd_routes.shape[2]
    width = fwd_tokens.shape[2]
    capacity = min(tokens, max(6, (tokens * topk + experts - 1) // experts + 2))
    w_gate, w_up, w_down = gate_weight[0], up_weight[0], down_weight[0]
    member_f, weight_f = route_tables(fwd_routes[0], fwd_scores[0], capacity, experts)
    member_b, weight_b = route_tables(bwd_routes[0], bwd_scores[0], capacity, experts)
    send_f = pick_rows(member_f, fwd_tokens[0])
    send_x = pick_rows(member_b, bwd_tokens[0])
    route_grad = jnp.einsum(
        "te,td->ed", weight_b, out_grad[0].astype(jnp.float32), precision=lax.Precision.HIGHEST
    )
    send_g = route_grad.astype(jnp.bfloat16)
    payload = jnp.stack((send_f, send_x, send_g)).reshape(3, experts, capacity, width)
    crossed = lax.all_to_all(payload, "eg", split_axis=1, concat_axis=1, tiled=True)
    arrived = lax.all_gather(crossed, "ei", axis=1, tiled=False)
    rows = arrived.reshape(3, -1, width)
    out_f = expert_forward(rows[0], w_gate, w_up, w_down)
    out_b = expert_backward(rows[1], rows[2], w_gate, w_up, w_down)
    parts = jnp.stack((out_f, out_b)).reshape((2,) + arrived.shape[1:])
    summed = lax.psum_scatter(parts, "ei", scatter_dimension=1, tiled=True)
    summed = summed.reshape(2, experts, capacity, width)
    home = lax.all_to_all(summed, "eg", split_axis=1, concat_axis=1, tiled=True)
    home = home.reshape(2, experts * capacity, width).astype(jnp.float32)
    layer_out = jnp.dot(weight_f, home[0], precision=lax.Precision.HIGHEST).astype(jnp.bfloat16)[
        None
    ]
    input_grad = jnp.dot(member_b, home[1], precision=lax.Precision.HIGHEST).astype(jnp.bfloat16)[
        None
    ]
    next_input = from_behind(layer_out, "pipe", 1)
    prev_grad = from_behind(input_grad, "pipe", -1)
    return (next_input, prev_grad)


def solution(mesh):
    pipe, expert = mesh.devices.shape
    split = Mesh(mesh.devices.reshape(pipe, expert // GROUP, GROUP), ("pipe", "eg", "ei"))
    rows = P("pipe", ("eg", "ei"), None)
    cols = P("pipe", None, ("eg", "ei"))
    placed = (rows, rows, rows, rows, rows, rows, rows, cols, cols, rows)
    return jax.shard_map(
        body,
        mesh=split,
        in_specs=placed,
        out_specs=(rows, rows),
        check_vma=False,
    )
```

```python
import jax
import jax.numpy as jnp
from jax import lax
from jax.sharding import Mesh
from jax.sharding import PartitionSpec as P

GROUP = 8


def from_behind(value, axis, steps):
    count = lax.axis_size(axis)
    pairs = [(source, (source + steps) % count) for source in range(count)]
    return lax.ppermute(value, axis, pairs)


def route_tables(routes, scores, capacity, experts):
    tokens, topk = routes.shape
    flat = routes.reshape(-1)
    onehot = (flat[:, None] == jnp.arange(experts, dtype=jnp.int32)[None, :]).astype(jnp.int32)
    rank = jnp.cumsum(onehot, axis=0) - onehot
    within = jnp.sum(rank * onehot, axis=1)
    slot_ids = (flat * capacity + within).reshape(tokens, topk)
    places = jnp.arange(experts * capacity, dtype=jnp.int32)
    hits = (slot_ids[:, :, None] == places[None, None, :]).astype(jnp.float32)
    normed = scores / jnp.sum(scores, axis=1, keepdims=True)
    member = jnp.sum(hits, axis=1)
    weighted = jnp.sum(hits * normed[:, :, None], axis=1)
    return (member, weighted)


def pick_rows(member, rows):
    slots = jnp.einsum(
        "te,td->ed", member.astype(jnp.bfloat16), rows, preferred_element_type=jnp.float32
    )
    return slots.astype(jnp.bfloat16)


def expert_forward(flat, w_gate, w_up, w_down):
    first = jnp.dot(flat, w_gate, preferred_element_type=jnp.float32)
    second = jnp.dot(flat, w_up, preferred_element_type=jnp.float32)
    hidden = (jax.nn.silu(first) * second).astype(jnp.bfloat16)
    return jnp.dot(hidden, w_down, preferred_element_type=jnp.float32).astype(jnp.bfloat16)


def expert_backward(flat, grads, w_gate, w_up, w_down):
    first = jnp.dot(flat, w_gate, preferred_element_type=jnp.float32)
    second = jnp.dot(flat, w_up, preferred_element_type=jnp.float32)
    d_hidden = lax.dot_general(
        grads, w_down, (((1,), (1,)), ((), ())), preferred_element_type=jnp.float32
    )
    sigm = 1.0 / (1.0 + jnp.exp(-first))
    d_first = (d_hidden * second * sigm * (1.0 + first * (1.0 - sigm))).astype(jnp.bfloat16)
    d_second = (d_hidden * first * sigm).astype(jnp.bfloat16)
    back = lax.dot_general(
        d_first, w_gate, (((1,), (1,)), ((), ())), preferred_element_type=jnp.float32
    )
    back = back + lax.dot_general(
        d_second, w_up, (((1,), (1,)), ((), ())), preferred_element_type=jnp.float32
    )
    return back.astype(jnp.bfloat16)


def body(
    fwd_tokens,
    fwd_routes,
    fwd_scores,
    bwd_tokens,
    bwd_routes,
    bwd_scores,
    out_grad,
    gate_weight,
    up_weight,
    down_weight,
):
    experts = lax.axis_size("eg")
    tokens = fwd_tokens.shape[1]
    topk = fwd_routes.shape[2]
    width = fwd_tokens.shape[2]
    capacity = min(tokens, max(6, (tokens * topk + experts - 1) // experts + 2))
    w_gate, w_up, w_down = gate_weight[0], up_weight[0], down_weight[0]
    member_f, weight_f = route_tables(fwd_routes[0], fwd_scores[0], capacity, experts)
    member_b, weight_b = route_tables(bwd_routes[0], bwd_scores[0], capacity, experts)
    send_f = pick_rows(member_f, fwd_tokens[0])
    send_x = pick_rows(member_b, bwd_tokens[0])
    route_grad = jnp.einsum(
        "te,td->ed", weight_b, out_grad[0].astype(jnp.float32), precision=lax.Precision.HIGHEST
    )
    send_g = route_grad.astype(jnp.bfloat16)
    lanes = 128
    payload = jnp.stack((send_f, send_x, send_g)).reshape(3, experts, -1, lanes)
    crossed = lax.all_to_all(payload, "eg", split_axis=1, concat_axis=1, tiled=True)
    arrived = lax.all_gather(crossed, "p", axis=1, tiled=False)
    arrived = lax.all_gather(arrived, "c", axis=2, tiled=False)
    rows = arrived.reshape(3, -1, width)
    out_f = expert_forward(rows[0], w_gate, w_up, w_down)
    out_b = expert_backward(rows[1], rows[2], w_gate, w_up, w_down)
    parts = jnp.stack((out_f, out_b)).reshape(2, arrived.shape[1], arrived.shape[2], experts, capacity, width)
    summed = lax.psum_scatter(parts, "c", scatter_dimension=2, tiled=True)
    summed = lax.psum_scatter(summed, "p", scatter_dimension=1, tiled=True)
    summed = summed.reshape(2, experts, -1, lanes)
    home = lax.all_to_all(summed, "eg", split_axis=1, concat_axis=1, tiled=True)
    home = home.reshape(2, experts * capacity, width).astype(jnp.float32)
    layer_out = jnp.dot(weight_f, home[0], precision=lax.Precision.HIGHEST).astype(jnp.bfloat16)[
        None
    ]
    input_grad = jnp.dot(member_b, home[1], precision=lax.Precision.HIGHEST).astype(jnp.bfloat16)[
        None
    ]
    next_input = from_behind(layer_out, "pipe", 1)
    prev_grad = from_behind(input_grad, "pipe", -1)
    return (next_input, prev_grad)


def solution(mesh):
    pipe, expert = mesh.devices.shape
    shape = (pipe, expert // GROUP, GROUP // 2, 2)
    split = Mesh(mesh.devices.reshape(shape), ("pipe", "eg", "p", "c"))
    rows = P("pipe", ("eg", "p", "c"), None)
    cols = P("pipe", None, ("eg", "p", "c"))
    placed = (rows, rows, rows, rows, rows, rows, rows, cols, cols, rows)
    return jax.shard_map(
        body,
        mesh=split,
        in_specs=placed,
        out_specs=(rows, rows),
        check_vma=False,
    )
```

```python
import jax
import jax.numpy as jnp
from jax import lax
from jax.sharding import Mesh
from jax.sharding import PartitionSpec as P

GROUP = 8


def from_behind(value, axis, steps):
    count = lax.axis_size(axis)
    pairs = [(source, (source + steps) % count) for source in range(count)]
    return lax.ppermute(value, axis, pairs)


def route_tables(routes, scores, capacity, experts):
    tokens, topk = routes.shape
    flat = routes.reshape(-1)
    onehot = (flat[:, None] == jnp.arange(experts, dtype=jnp.int32)[None, :]).astype(jnp.int32)
    rank = jnp.cumsum(onehot, axis=0) - onehot
    within = jnp.sum(rank * onehot, axis=1)
    slot_ids = (flat * capacity + within).reshape(tokens, topk)
    places = jnp.arange(experts * capacity, dtype=jnp.int32)
    hits = (slot_ids[:, :, None] == places[None, None, :]).astype(jnp.float32)
    normed = scores / jnp.sum(scores, axis=1, keepdims=True)
    member = jnp.sum(hits, axis=1)
    weighted = jnp.sum(hits * normed[:, :, None], axis=1)
    return (member, weighted)


def pick_rows(member, rows):
    slots = jnp.einsum(
        "te,td->ed", member.astype(jnp.bfloat16), rows, preferred_element_type=jnp.float32
    )
    return slots.astype(jnp.bfloat16)


def expert_pair(rows, grads, w_gate, w_up, w_down):
    count = grads.shape[0]
    hid = w_gate.shape[1]
    both = jnp.dot(rows, jnp.concatenate((w_gate, w_up), axis=1), preferred_element_type=jnp.float32)
    first, second = both[:, :hid], both[:, hid:]
    hidden = (jax.nn.silu(first[:count]) * second[:count]).astype(jnp.bfloat16)
    d_hidden = lax.dot_general(
        grads, w_down, (((1,), (1,)), ((), ())), preferred_element_type=jnp.float32
    )
    a, b = first[count:], second[count:]
    sigm = 1.0 / (1.0 + jnp.exp(-a))
    d_first = (d_hidden * b * sigm * (1.0 + a * (1.0 - sigm))).astype(jnp.bfloat16)
    d_second = (d_hidden * a * sigm).astype(jnp.bfloat16)
    zero = jnp.zeros_like(hidden)
    left = jnp.concatenate(
        (
            jnp.concatenate((hidden, zero, zero), axis=1),
            jnp.concatenate((zero, d_first, d_second), axis=1),
        ),
        axis=0,
    )
    right = jnp.concatenate((w_down, w_gate.T, w_up.T), axis=0)
    return jnp.dot(left, right, preferred_element_type=jnp.float32).astype(jnp.bfloat16)


def body(
    fwd_tokens,
    fwd_routes,
    fwd_scores,
    bwd_tokens,
    bwd_routes,
    bwd_scores,
    out_grad,
    gate_weight,
    up_weight,
    down_weight,
):
    experts = lax.axis_size("eg")
    tokens = fwd_tokens.shape[1]
    topk = fwd_routes.shape[2]
    width = fwd_tokens.shape[2]
    capacity = min(tokens, max(6, (tokens * topk + experts - 1) // experts + 2))
    w_gate, w_up, w_down = gate_weight[0], up_weight[0], down_weight[0]
    member_f, weight_f = route_tables(fwd_routes[0], fwd_scores[0], capacity, experts)
    member_b, weight_b = route_tables(bwd_routes[0], bwd_scores[0], capacity, experts)
    send_f = pick_rows(member_f, fwd_tokens[0])
    send_x = pick_rows(member_b, bwd_tokens[0])
    route_grad = jnp.einsum(
        "te,td->ed", weight_b, out_grad[0].astype(jnp.float32), precision=lax.Precision.HIGHEST
    )
    send_g = route_grad.astype(jnp.bfloat16)
    lanes = 128
    payload = jnp.stack((send_f, send_x, send_g)).reshape(3, experts, -1, lanes)
    crossed = lax.all_to_all(payload, "eg", split_axis=1, concat_axis=1, tiled=True)
    crossed = crossed.reshape(3, experts, capacity, width).transpose(0, 2, 1, 3)
    arrived = lax.all_gather(crossed, "ei", axis=1, tiled=False)
    rows = arrived.reshape(3, -1, width)
    parts = expert_pair(rows[:2].reshape(-1, width), rows[2], w_gate, w_up, w_down)
    parts = parts.reshape((2,) + arrived.shape[1:])
    summed = lax.psum_scatter(parts, "ei", scatter_dimension=1, tiled=True)
    summed = summed.reshape(2, capacity, experts, width).transpose(0, 2, 1, 3)
    summed = summed.reshape(2, experts, -1, lanes)
    home = lax.all_to_all(summed, "eg", split_axis=1, concat_axis=1, tiled=True)
    home = home.reshape(2, experts * capacity, width).astype(jnp.float32)
    layer_out = jnp.dot(weight_f, home[0], precision=lax.Precision.HIGHEST).astype(jnp.bfloat16)[
        None
    ]
    input_grad = jnp.dot(member_b, home[1], precision=lax.Precision.HIGHEST).astype(jnp.bfloat16)[
        None
    ]
    next_input = from_behind(layer_out, "pipe", 1)
    prev_grad = from_behind(input_grad, "pipe", -1)
    return (next_input, prev_grad)


def solution(mesh):
    pipe, expert = mesh.devices.shape
    split = Mesh(mesh.devices.reshape(pipe, expert // GROUP, GROUP), ("pipe", "eg", "ei"))
    rows = P("pipe", ("eg", "ei"), None)
    cols = P("pipe", None, ("eg", "ei"))
    placed = (rows, rows, rows, rows, rows, rows, rows, cols, cols, rows)
    return jax.shard_map(
        body,
        mesh=split,
        in_specs=placed,
        out_specs=(rows, rows),
        check_vma=False,
    )
```

```python
import jax
import jax.numpy as jnp
from jax import lax
from jax.sharding import Mesh
from jax.sharding import PartitionSpec as P

GROUP = 8


def from_behind(value, axis, steps):
    count = lax.axis_size(axis)
    pairs = [(source, (source + steps) % count) for source in range(count)]
    return lax.ppermute(value, axis, pairs)


def route_tables(routes, scores, capacity, experts):
    tokens, topk = routes.shape
    flat = routes.reshape(-1)
    onehot = (flat[:, None] == jnp.arange(experts, dtype=jnp.int32)[None, :]).astype(jnp.int32)
    rank = jnp.cumsum(onehot, axis=0) - onehot
    within = jnp.sum(rank * onehot, axis=1)
    slot_ids = (flat * capacity + within).reshape(tokens, topk)
    places = jnp.arange(experts * capacity, dtype=jnp.int32)
    hits = (slot_ids[:, :, None] == places[None, None, :]).astype(jnp.float32)
    normed = scores / jnp.sum(scores, axis=1, keepdims=True)
    member = jnp.sum(hits, axis=1)
    weighted = jnp.sum(hits * normed[:, :, None], axis=1)
    return (member, weighted)


def pick_rows(member, rows):
    slots = jnp.einsum(
        "te,td->ed", member.astype(jnp.bfloat16), rows, preferred_element_type=jnp.float32
    )
    return slots.astype(jnp.bfloat16)


def expert_forward(rows, w_gate, w_up, w_down):
    first = jnp.dot(rows, w_gate, preferred_element_type=jnp.float32)
    second = jnp.dot(rows, w_up, preferred_element_type=jnp.float32)
    hidden = (jax.nn.silu(first) * second).astype(jnp.bfloat16)
    return jnp.dot(hidden, w_down, preferred_element_type=jnp.float32).astype(jnp.bfloat16)


def expert_backward(rows, grads, w_gate, w_up, w_down):
    hid = w_gate.shape[1]
    both = jnp.dot(rows, jnp.concatenate((w_gate, w_up), axis=1), preferred_element_type=jnp.float32)
    a, b = both[:, :hid], both[:, hid:]
    d_hidden = lax.dot_general(
        grads, w_down, (((1,), (1,)), ((), ())), preferred_element_type=jnp.float32
    )
    sigm = 1.0 / (1.0 + jnp.exp(-a))
    d_first = (d_hidden * b * sigm * (1.0 + a * (1.0 - sigm))).astype(jnp.bfloat16)
    d_second = (d_hidden * a * sigm).astype(jnp.bfloat16)
    left = jnp.concatenate((d_first, d_second), axis=1)
    right = jnp.concatenate((w_gate.T, w_up.T), axis=0)
    return jnp.dot(left, right, preferred_element_type=jnp.float32).astype(jnp.bfloat16)


def dispatch(payload, capacity, width):
    kinds, experts = payload.shape[:2]
    crossed = lax.all_to_all(payload, "eg", split_axis=1, concat_axis=1, tiled=True)
    crossed = crossed.reshape(kinds, experts, capacity, width).transpose(0, 2, 1, 3)
    return lax.all_gather(crossed, "ei", axis=1, tiled=False)


def collect(parts, lanes):
    kinds, _, capacity, experts, width = parts.shape
    summed = lax.psum_scatter(parts, "ei", scatter_dimension=1, tiled=True)
    summed = summed.reshape(kinds, capacity, experts, width).transpose(0, 2, 1, 3)
    summed = summed.reshape(kinds, experts, -1, lanes)
    home = lax.all_to_all(summed, "eg", split_axis=1, concat_axis=1, tiled=True)
    return home.reshape(kinds, experts * capacity, width).astype(jnp.float32)


def body(
    fwd_tokens,
    fwd_routes,
    fwd_scores,
    bwd_tokens,
    bwd_routes,
    bwd_scores,
    out_grad,
    gate_weight,
    up_weight,
    down_weight,
):
    experts = lax.axis_size("eg")
    tokens = fwd_tokens.shape[1]
    topk = fwd_routes.shape[2]
    width = fwd_tokens.shape[2]
    capacity = min(tokens, max(6, (tokens * topk + experts - 1) // experts + 2))
    w_gate, w_up, w_down = gate_weight[0], up_weight[0], down_weight[0]
    member_f, weight_f = route_tables(fwd_routes[0], fwd_scores[0], capacity, experts)
    member_b, weight_b = route_tables(bwd_routes[0], bwd_scores[0], capacity, experts)
    send_f = pick_rows(member_f, fwd_tokens[0])
    send_x = pick_rows(member_b, bwd_tokens[0])
    route_grad = jnp.einsum(
        "te,td->ed", weight_b, out_grad[0].astype(jnp.float32), precision=lax.Precision.HIGHEST
    )
    send_g = route_grad.astype(jnp.bfloat16)
    lanes = 128
    arrived_b = dispatch(jnp.stack((send_x, send_g)).reshape(2, experts, -1, lanes), capacity, width)
    arrived_f = dispatch(send_f.reshape(1, experts, -1, lanes), capacity, width)
    grid = arrived_f.shape
    rows_b = arrived_b.reshape(2, -1, width)
    out_b = expert_backward(rows_b[0], rows_b[1], w_gate, w_up, w_down)
    out_f = expert_forward(arrived_f.reshape(-1, width), w_gate, w_up, w_down)
    home_b = collect(out_b.reshape(grid), lanes)
    home_f = collect(out_f.reshape(grid), lanes)
    home = (home_f[0], home_b[0])
    layer_out = jnp.dot(weight_f, home[0], precision=lax.Precision.HIGHEST).astype(jnp.bfloat16)[
        None
    ]
    input_grad = jnp.dot(member_b, home[1], precision=lax.Precision.HIGHEST).astype(jnp.bfloat16)[
        None
    ]
    next_input = from_behind(layer_out, "pipe", 1)
    prev_grad = from_behind(input_grad, "pipe", -1)
    return (next_input, prev_grad)


def solution(mesh):
    pipe, expert = mesh.devices.shape
    split = Mesh(mesh.devices.reshape(pipe, expert // GROUP, GROUP), ("pipe", "eg", "ei"))
    rows = P("pipe", ("eg", "ei"), None)
    cols = P("pipe", None, ("eg", "ei"))
    placed = (rows, rows, rows, rows, rows, rows, rows, cols, cols, rows)
    return jax.shard_map(
        body,
        mesh=split,
        in_specs=placed,
        out_specs=(rows, rows),
        check_vma=False,
    )
```

```python
import jax
import jax.numpy as jnp
from jax import lax
from jax.sharding import Mesh
from jax.sharding import PartitionSpec as P

GROUP = 8


def from_behind(value, axis, steps):
    count = lax.axis_size(axis)
    pairs = [(source, (source + steps) % count) for source in range(count)]
    return lax.ppermute(value, axis, pairs)


def route_tables(routes, scores, capacity, experts):
    tokens, topk = routes.shape
    flat = routes.reshape(-1)
    onehot = (flat[:, None] == jnp.arange(experts, dtype=jnp.int32)[None, :]).astype(jnp.int32)
    rank = jnp.cumsum(onehot, axis=0) - onehot
    within = jnp.sum(rank * onehot, axis=1)
    slot_ids = (flat * capacity + within).reshape(tokens, topk)
    places = jnp.arange(experts * capacity, dtype=jnp.int32)
    hits = (slot_ids[:, :, None] == places[None, None, :]).astype(jnp.float32)
    normed = scores / jnp.sum(scores, axis=1, keepdims=True)
    member = jnp.sum(hits, axis=1)
    weighted = jnp.sum(hits * normed[:, :, None], axis=1)
    return (member, weighted)


def pick_rows(member, rows):
    slots = jnp.einsum(
        "te,td->ed", member.astype(jnp.bfloat16), rows, preferred_element_type=jnp.float32
    )
    return slots.astype(jnp.bfloat16)


def expert_pair(rows, grads, w_gate, w_up, w_down):
    count = grads.shape[0]
    hid = w_gate.shape[1]
    both = jnp.dot(rows, jnp.concatenate((w_gate, w_up), axis=1), preferred_element_type=jnp.float32)
    first, second = both[:, :hid], both[:, hid:]
    hidden = (jax.nn.silu(first[:count]) * second[:count]).astype(jnp.bfloat16)
    d_hidden = lax.dot_general(
        grads, w_down, (((1,), (1,)), ((), ())), preferred_element_type=jnp.float32
    )
    a, b = first[count:], second[count:]
    sigm = 1.0 / (1.0 + jnp.exp(-a))
    d_first = (d_hidden * b * sigm * (1.0 + a * (1.0 - sigm))).astype(jnp.bfloat16)
    d_second = (d_hidden * a * sigm).astype(jnp.bfloat16)
    zero = jnp.zeros_like(hidden)
    left = jnp.concatenate(
        (
            jnp.concatenate((hidden, zero, zero), axis=1),
            jnp.concatenate((zero, d_first, d_second), axis=1),
        ),
        axis=0,
    )
    right = jnp.concatenate((w_down, w_gate.T, w_up.T), axis=0)
    return jnp.dot(left, right, preferred_element_type=jnp.float32).astype(jnp.bfloat16)


def body(
    fwd_tokens,
    fwd_routes,
    fwd_scores,
    bwd_tokens,
    bwd_routes,
    bwd_scores,
    out_grad,
    gate_weight,
    up_weight,
    down_weight,
):
    experts = lax.axis_size("eg")
    tokens = fwd_tokens.shape[1]
    topk = fwd_routes.shape[2]
    width = fwd_tokens.shape[2]
    capacity = min(tokens, max(6, (tokens * topk + experts - 1) // experts + 2))
    w_gate, w_up, w_down = gate_weight[0], up_weight[0], down_weight[0]
    member_f, weight_f = route_tables(fwd_routes[0], fwd_scores[0], capacity, experts)
    member_b, weight_b = route_tables(bwd_routes[0], bwd_scores[0], capacity, experts)
    send_f = pick_rows(member_f, fwd_tokens[0])
    send_x = pick_rows(member_b, bwd_tokens[0])
    route_grad = jnp.einsum(
        "te,td->ed", weight_b, out_grad[0].astype(jnp.float32), precision=lax.Precision.HIGHEST
    )
    send_g = route_grad.astype(jnp.bfloat16)
    lanes = 128
    payload = jnp.stack((send_f, send_x, send_g)).reshape(3, experts, -1, lanes)
    crossed = lax.all_to_all(payload, "eg", split_axis=1, concat_axis=1, tiled=True)
    crossed = crossed.reshape(3, experts, capacity, width).transpose(0, 2, 1, 3)
    arrived = lax.all_gather(crossed, "ei", axis=1, tiled=False)
    rows = arrived.reshape(3, -1, width)
    parts = expert_pair(rows[:2].reshape(-1, width), rows[2], w_gate, w_up, w_down)
    parts = parts.reshape(2, arrived.shape[1], -1, width)
    summed = lax.psum_scatter(parts, "ei", scatter_dimension=1, tiled=True)
    summed = summed.reshape(2, capacity, experts, width).transpose(0, 2, 1, 3)
    summed = summed.reshape(2, experts, -1, lanes)
    home = lax.all_to_all(summed, "eg", split_axis=1, concat_axis=1, tiled=True)
    home = home.reshape(2, experts * capacity, width).astype(jnp.float32)
    layer_out = jnp.dot(weight_f, home[0], precision=lax.Precision.HIGHEST).astype(jnp.bfloat16)[
        None
    ]
    input_grad = jnp.dot(member_b, home[1], precision=lax.Precision.HIGHEST).astype(jnp.bfloat16)[
        None
    ]
    next_input = from_behind(layer_out, "pipe", 1)
    prev_grad = from_behind(input_grad, "pipe", -1)
    return (next_input, prev_grad)


def solution(mesh):
    pipe, expert = mesh.devices.shape
    split = Mesh(mesh.devices.reshape(pipe, expert // GROUP, GROUP), ("pipe", "eg", "ei"))
    rows = P("pipe", ("eg", "ei"), None)
    cols = P("pipe", None, ("eg", "ei"))
    placed = (rows, rows, rows, rows, rows, rows, rows, cols, cols, rows)
    return jax.shard_map(
        body,
        mesh=split,
        in_specs=placed,
        out_specs=(rows, rows),
        check_vma=False,
    )
```

```python
import jax
import jax.numpy as jnp
from jax import lax
from jax.sharding import Mesh
from jax.sharding import PartitionSpec as P

GROUP = 8


def from_behind(value, axis, steps):
    count = lax.axis_size(axis)
    pairs = [(source, (source + steps) % count) for source in range(count)]
    return lax.ppermute(value, axis, pairs)


def route_tables(routes, scores, capacity, experts):
    tokens, topk = routes.shape
    flat = (routes.reshape(-1) - lax.axis_index("eg")) % experts
    onehot = (flat[:, None] == jnp.arange(experts, dtype=jnp.int32)[None, :]).astype(jnp.int32)
    rank = jnp.cumsum(onehot, axis=0) - onehot
    within = jnp.sum(rank * onehot, axis=1)
    slot_ids = (flat * capacity + within).reshape(tokens, topk)
    places = jnp.arange(experts * capacity, dtype=jnp.int32)
    hits = (slot_ids[:, :, None] == places[None, None, :]).astype(jnp.float32)
    normed = scores / jnp.sum(scores, axis=1, keepdims=True)
    member = jnp.sum(hits, axis=1)
    weighted = jnp.sum(hits * normed[:, :, None], axis=1)
    return (member, weighted)


def pick_rows(member, rows):
    slots = jnp.einsum(
        "te,td->ed", member.astype(jnp.bfloat16), rows, preferred_element_type=jnp.float32
    )
    return slots.astype(jnp.bfloat16)


def expert_pair(rows, grads, w_gate, w_up, w_down):
    count = grads.shape[0]
    hid = w_gate.shape[1]
    both = jnp.dot(rows, jnp.concatenate((w_gate, w_up), axis=1), preferred_element_type=jnp.float32)
    first, second = both[:, :hid], both[:, hid:]
    hidden = (jax.nn.silu(first[:count]) * second[:count]).astype(jnp.bfloat16)
    d_hidden = lax.dot_general(
        grads, w_down, (((1,), (1,)), ((), ())), preferred_element_type=jnp.float32
    )
    a, b = first[count:], second[count:]
    sigm = 1.0 / (1.0 + jnp.exp(-a))
    d_first = (d_hidden * b * sigm * (1.0 + a * (1.0 - sigm))).astype(jnp.bfloat16)
    d_second = (d_hidden * a * sigm).astype(jnp.bfloat16)
    zero = jnp.zeros_like(hidden)
    left = jnp.concatenate(
        (
            jnp.concatenate((hidden, zero, zero), axis=1),
            jnp.concatenate((zero, d_first, d_second), axis=1),
        ),
        axis=0,
    )
    right = jnp.concatenate((w_down, w_gate.T, w_up.T), axis=0)
    return jnp.dot(left, right, preferred_element_type=jnp.float32).astype(jnp.bfloat16)


def exchange(blocks, steps):
    count = blocks.shape[1]
    moved = [blocks[:, 0]]
    for k in range(1, count):
        pairs = [(source, (source + steps * k) % count) for source in range(count)]
        moved.append(lax.ppermute(blocks[:, k], "eg", pairs))
    return jnp.stack(moved, axis=1)


def body(
    fwd_tokens,
    fwd_routes,
    fwd_scores,
    bwd_tokens,
    bwd_routes,
    bwd_scores,
    out_grad,
    gate_weight,
    up_weight,
    down_weight,
):
    experts = lax.axis_size("eg")
    tokens = fwd_tokens.shape[1]
    topk = fwd_routes.shape[2]
    width = fwd_tokens.shape[2]
    capacity = min(tokens, max(6, (tokens * topk + experts - 1) // experts + 2))
    w_gate, w_up, w_down = gate_weight[0], up_weight[0], down_weight[0]
    member_f, weight_f = route_tables(fwd_routes[0], fwd_scores[0], capacity, experts)
    member_b, weight_b = route_tables(bwd_routes[0], bwd_scores[0], capacity, experts)
    send_f = pick_rows(member_f, fwd_tokens[0])
    send_x = pick_rows(member_b, bwd_tokens[0])
    route_grad = jnp.einsum(
        "te,td->ed", weight_b, out_grad[0].astype(jnp.float32), precision=lax.Precision.HIGHEST
    )
    send_g = route_grad.astype(jnp.bfloat16)
    lanes = 128
    payload = jnp.stack((send_f, send_x, send_g)).reshape(3, experts, -1, lanes)
    crossed = exchange(payload, 1)
    crossed = crossed.reshape(3, experts, capacity, width).transpose(0, 2, 1, 3)
    arrived = lax.all_gather(crossed, "ei", axis=1, tiled=False)
    rows = arrived.reshape(3, -1, width)
    parts = expert_pair(rows[:2].reshape(-1, width), rows[2], w_gate, w_up, w_down)
    parts = parts.reshape(2, arrived.shape[1], -1, width)
    summed = lax.psum_scatter(parts, "ei", scatter_dimension=1, tiled=True)
    summed = summed.reshape(2, capacity, experts, width).transpose(0, 2, 1, 3)
    summed = summed.reshape(2, experts, -1, lanes)
    home = exchange(summed, -1)
    home = home.reshape(2, experts * capacity, width).astype(jnp.float32)
    layer_out = jnp.dot(weight_f, home[0], precision=lax.Precision.HIGHEST).astype(jnp.bfloat16)[
        None
    ]
    input_grad = jnp.dot(member_b, home[1], precision=lax.Precision.HIGHEST).astype(jnp.bfloat16)[
        None
    ]
    next_input = from_behind(layer_out, "pipe", 1)
    prev_grad = from_behind(input_grad, "pipe", -1)
    return (next_input, prev_grad)


def solution(mesh):
    pipe, expert = mesh.devices.shape
    split = Mesh(mesh.devices.reshape(pipe, expert // GROUP, GROUP), ("pipe", "eg", "ei"))
    rows = P("pipe", ("eg", "ei"), None)
    cols = P("pipe", None, ("eg", "ei"))
    placed = (rows, rows, rows, rows, rows, rows, rows, cols, cols, rows)
    return jax.shard_map(
        body,
        mesh=split,
        in_specs=placed,
        out_specs=(rows, rows),
        check_vma=False,
    )
```

```python
import jax
import jax.numpy as jnp
from jax import lax
from jax.sharding import Mesh
from jax.sharding import PartitionSpec as P

GROUP = 8


def from_behind(value, axis, steps):
    count = lax.axis_size(axis)
    pairs = [(source, (source + steps) % count) for source in range(count)]
    return lax.ppermute(value, axis, pairs)


def route_tables(routes, scores, capacity, experts):
    tokens, topk = routes.shape
    flat = routes.reshape(-1)
    onehot = (flat[:, None] == jnp.arange(experts, dtype=jnp.int32)[None, :]).astype(jnp.int32)
    rank = jnp.cumsum(onehot, axis=0) - onehot
    within = jnp.sum(rank * onehot, axis=1)
    slot_ids = (flat * capacity + within).reshape(tokens, topk)
    places = jnp.arange(experts * capacity, dtype=jnp.int32)
    hits = (slot_ids[:, :, None] == places[None, None, :]).astype(jnp.float32)
    normed = scores / jnp.sum(scores, axis=1, keepdims=True)
    member = jnp.sum(hits, axis=1)
    weighted = jnp.sum(hits * normed[:, :, None], axis=1)
    return (member, weighted)


def pick_rows(member, rows):
    slots = jnp.einsum(
        "te,td->ed", member.astype(jnp.bfloat16), rows, preferred_element_type=jnp.float32
    )
    return slots.astype(jnp.bfloat16)


def expert_pair(rows, grads, w_gate, w_up, w_down):
    count = grads.shape[0]
    hid = w_gate.shape[1]
    both = jnp.dot(rows, jnp.concatenate((w_gate, w_up), axis=1), preferred_element_type=jnp.float32)
    first, second = both[:, :hid], both[:, hid:]
    hidden = (jax.nn.silu(first[:count]) * second[:count]).astype(jnp.bfloat16)
    d_hidden = lax.dot_general(
        grads, w_down, (((1,), (1,)), ((), ())), preferred_element_type=jnp.float32
    )
    a, b = first[count:], second[count:]
    sigm = 1.0 / (1.0 + jnp.exp(-a))
    d_first = (d_hidden * b * sigm * (1.0 + a * (1.0 - sigm))).astype(jnp.bfloat16)
    d_second = (d_hidden * a * sigm).astype(jnp.bfloat16)
    zero = jnp.zeros_like(hidden)
    left = jnp.concatenate(
        (
            jnp.concatenate((hidden, zero, zero), axis=1),
            jnp.concatenate((zero, d_first, d_second), axis=1),
        ),
        axis=0,
    )
    right = jnp.concatenate((w_down, w_gate.T, w_up.T), axis=0)
    return jnp.dot(left, right, preferred_element_type=jnp.float32).astype(jnp.bfloat16)


def body(
    fwd_tokens,
    fwd_routes,
    fwd_scores,
    bwd_tokens,
    bwd_routes,
    bwd_scores,
    out_grad,
    gate_weight,
    up_weight,
    down_weight,
):
    experts = lax.axis_size("eg")
    tokens = fwd_tokens.shape[1]
    topk = fwd_routes.shape[2]
    width = fwd_tokens.shape[2]
    capacity = min(tokens, max(6, (tokens * topk + experts - 1) // experts + 2))
    swap = [(0, 1), (1, 0)]
    own = (gate_weight[0], up_weight[0], down_weight[0])
    other = tuple(lax.ppermute(w, "c", swap) for w in own)
    w_gate = jnp.concatenate((own[0], other[0]), axis=1)
    w_up = jnp.concatenate((own[1], other[1]), axis=1)
    w_down = jnp.concatenate((own[2], other[2]), axis=0)
    member_f, weight_f = route_tables(fwd_routes[0], fwd_scores[0], capacity, experts)
    member_b, weight_b = route_tables(bwd_routes[0], bwd_scores[0], capacity, experts)
    send_f = pick_rows(member_f, fwd_tokens[0])
    send_x = pick_rows(member_b, bwd_tokens[0])
    route_grad = jnp.einsum(
        "te,td->ed", weight_b, out_grad[0].astype(jnp.float32), precision=lax.Precision.HIGHEST
    )
    send_g = route_grad.astype(jnp.bfloat16)
    lanes = 128
    payload = jnp.stack((send_f, send_x, send_g)).reshape(3, experts, -1, lanes)
    crossed = lax.all_to_all(payload, "eg", split_axis=1, concat_axis=1, tiled=True)
    crossed = crossed.reshape(3, experts, capacity, width).transpose(0, 2, 1, 3)
    arrived = lax.all_gather(crossed, "p", axis=1, tiled=False)
    rows = arrived.reshape(3, -1, width)
    parts = expert_pair(rows[:2].reshape(-1, width), rows[2], w_gate, w_up, w_down)
    parts = parts.reshape(2, arrived.shape[1], -1, width)
    summed = lax.psum_scatter(parts, "p", scatter_dimension=1, tiled=True)
    summed = summed.reshape(2, capacity, experts, width).transpose(0, 2, 1, 3)
    summed = summed.reshape(2, experts, -1, lanes)
    home = lax.all_to_all(summed, "eg", split_axis=1, concat_axis=1, tiled=True)
    home = home.reshape(2, experts * capacity, width).astype(jnp.float32)
    layer_out = jnp.dot(weight_f, home[0], precision=lax.Precision.HIGHEST).astype(jnp.bfloat16)[
        None
    ]
    input_grad = jnp.dot(member_b, home[1], precision=lax.Precision.HIGHEST).astype(jnp.bfloat16)[
        None
    ]
    next_input = from_behind(layer_out, "pipe", 1)
    prev_grad = from_behind(input_grad, "pipe", -1)
    return (next_input, prev_grad)


def solution(mesh):
    pipe, expert = mesh.devices.shape
    shape = (pipe, expert // GROUP, GROUP // 2, 2)
    split = Mesh(mesh.devices.reshape(shape), ("pipe", "eg", "p", "c"))
    rows = P("pipe", ("eg", "p", "c"), None)
    cols = P("pipe", None, ("eg", "p", "c"))
    placed = (rows, rows, rows, rows, rows, rows, rows, cols, cols, rows)
    return jax.shard_map(
        body,
        mesh=split,
        in_specs=placed,
        out_specs=(rows, rows),
        check_vma=False,
    )
```

```python
import jax
import jax.numpy as jnp
from jax import lax
from jax.sharding import Mesh
from jax.sharding import PartitionSpec as P

GROUP = 8


def from_behind(value, axis, steps):
    count = lax.axis_size(axis)
    pairs = [(source, (source + steps) % count) for source in range(count)]
    return lax.ppermute(value, axis, pairs)


def route_tables(routes, scores, capacity, experts):
    kinds, tokens, topk = routes.shape
    flat = routes.reshape(kinds, -1)
    onehot = (flat[:, :, None] == jnp.arange(experts, dtype=jnp.int32)).astype(jnp.int32)
    rank = jnp.cumsum(onehot, axis=1) - onehot
    within = jnp.sum(rank * onehot, axis=2)
    slot_ids = (flat * capacity + within).reshape(kinds, tokens, topk)
    places = jnp.arange(experts * capacity, dtype=jnp.int32)
    hits = (slot_ids[..., None] == places).astype(jnp.float32)
    normed = scores / jnp.sum(scores, axis=2, keepdims=True)
    member = jnp.sum(hits, axis=2)
    weighted = jnp.sum(hits * normed[..., None], axis=2)
    return (member, weighted)


def pick_rows(member, rows):
    slots = jnp.einsum(
        "te,td->ed", member.astype(jnp.bfloat16), rows, preferred_element_type=jnp.float32
    )
    return slots.astype(jnp.bfloat16)


def expert_pair(rows, grads, w_gate, w_up, w_down):
    count = grads.shape[0]
    hid = w_gate.shape[1]
    both = jnp.dot(rows, jnp.concatenate((w_gate, w_up), axis=1), preferred_element_type=jnp.float32)
    first, second = both[:, :hid], both[:, hid:]
    hidden = (jax.nn.silu(first[:count]) * second[:count]).astype(jnp.bfloat16)
    d_hidden = lax.dot_general(
        grads, w_down, (((1,), (1,)), ((), ())), preferred_element_type=jnp.float32
    )
    a, b = first[count:], second[count:]
    sigm = 1.0 / (1.0 + jnp.exp(-a))
    d_first = (d_hidden * b * sigm * (1.0 + a * (1.0 - sigm))).astype(jnp.bfloat16)
    d_second = (d_hidden * a * sigm).astype(jnp.bfloat16)
    zero = jnp.zeros_like(hidden)
    left = jnp.concatenate(
        (
            jnp.concatenate((hidden, zero, zero), axis=1),
            jnp.concatenate((zero, d_first, d_second), axis=1),
        ),
        axis=0,
    )
    right = jnp.concatenate((w_down, w_gate.T, w_up.T), axis=0)
    return jnp.dot(left, right, preferred_element_type=jnp.float32).astype(jnp.bfloat16)


def body(
    fwd_tokens,
    fwd_routes,
    fwd_scores,
    bwd_tokens,
    bwd_routes,
    bwd_scores,
    out_grad,
    gate_weight,
    up_weight,
    down_weight,
):
    experts = lax.axis_size("eg")
    tokens = fwd_tokens.shape[1]
    topk = fwd_routes.shape[2]
    width = fwd_tokens.shape[2]
    capacity = min(tokens, max(6, (tokens * topk + experts - 1) // experts + 2))
    swap = [(0, 1), (1, 0)]
    own = (gate_weight[0], up_weight[0], down_weight[0])
    other = tuple(lax.ppermute(w, "c", swap) for w in own)
    w_gate = jnp.concatenate((own[0], other[0]), axis=1)
    w_up = jnp.concatenate((own[1], other[1]), axis=1)
    w_down = jnp.concatenate((own[2], other[2]), axis=0)
    member, weighted = route_tables(
        jnp.concatenate((fwd_routes, bwd_routes)),
        jnp.concatenate((fwd_scores, bwd_scores)),
        capacity,
        experts,
    )
    weight_f, member_b = weighted[0], member[1]
    pickers = jnp.stack((member[0], member_b, weighted[1]))
    sources = jnp.concatenate((fwd_tokens, bwd_tokens, out_grad)).astype(jnp.float32)
    chosen = jnp.einsum("kte,ktd->ked", pickers, sources, precision=lax.Precision.HIGHEST)
    lanes = 128
    payload = chosen.astype(jnp.bfloat16).reshape(3, experts, -1, lanes)
    crossed = lax.all_to_all(payload, "eg", split_axis=1, concat_axis=1, tiled=True)
    crossed = crossed.reshape(3, experts, capacity, width).transpose(0, 2, 1, 3)
    arrived = lax.all_gather(crossed, "p", axis=1, tiled=False)
    rows = arrived.reshape(3, -1, width)
    parts = expert_pair(rows[:2].reshape(-1, width), rows[2], w_gate, w_up, w_down)
    parts = parts.reshape(2, arrived.shape[1], -1, width)
    summed = lax.psum_scatter(parts, "p", scatter_dimension=1, tiled=True)
    summed = summed.reshape(2, capacity, experts, width).transpose(0, 2, 1, 3)
    summed = summed.reshape(2, experts, -1, lanes)
    home = lax.all_to_all(summed, "eg", split_axis=1, concat_axis=1, tiled=True)
    home = home.reshape(2, experts * capacity, width).astype(jnp.float32)
    layer_out = jnp.dot(weight_f, home[0], precision=lax.Precision.HIGHEST).astype(jnp.bfloat16)[
        None
    ]
    input_grad = jnp.dot(member_b, home[1], precision=lax.Precision.HIGHEST).astype(jnp.bfloat16)[
        None
    ]
    next_input = from_behind(layer_out, "pipe", 1)
    prev_grad = from_behind(input_grad, "pipe", -1)
    return (next_input, prev_grad)


def solution(mesh):
    pipe, expert = mesh.devices.shape
    shape = (pipe, expert // GROUP, GROUP // 2, 2)
    split = Mesh(mesh.devices.reshape(shape), ("pipe", "eg", "p", "c"))
    rows = P("pipe", ("eg", "p", "c"), None)
    cols = P("pipe", None, ("eg", "p", "c"))
    placed = (rows, rows, rows, rows, rows, rows, rows, cols, cols, rows)
    return jax.shard_map(
        body,
        mesh=split,
        in_specs=placed,
        out_specs=(rows, rows),
        check_vma=False,
    )
```

```python
import jax
import jax.numpy as jnp
from jax import lax
from jax.sharding import Mesh
from jax.sharding import PartitionSpec as P

GROUP = 8


def from_behind(value, axis, steps):
    count = lax.axis_size(axis)
    pairs = [(source, (source + steps) % count) for source in range(count)]
    return lax.ppermute(value, axis, pairs)


def route_tables(routes, scores, capacity, experts):
    kinds, tokens, topk = routes.shape
    flat = routes.reshape(kinds, -1)
    onehot = (flat[:, :, None] == jnp.arange(experts, dtype=jnp.int32)).astype(jnp.int32)
    rank = jnp.cumsum(onehot, axis=1) - onehot
    within = jnp.sum(rank * onehot, axis=2)
    slot_ids = (flat * capacity + within).reshape(kinds, tokens, topk)
    places = jnp.arange(experts * capacity, dtype=jnp.int32)
    hits = (slot_ids[..., None] == places).astype(jnp.float32)
    normed = scores / jnp.sum(scores, axis=2, keepdims=True)
    member = jnp.sum(hits, axis=2)
    weighted = jnp.sum(hits * normed[..., None], axis=2)
    return (member, weighted)


def pick_rows(member, rows):
    slots = jnp.einsum(
        "te,td->ed", member.astype(jnp.bfloat16), rows, preferred_element_type=jnp.float32
    )
    return slots.astype(jnp.bfloat16)


def expert_pair(mixed, grads, w_gate, w_up, w_down):
    count = grads.shape[0]
    hid = w_gate.shape[1]
    width = mixed.shape[-1]
    both = jnp.dot(
        mixed.reshape(-1, width),
        jnp.concatenate((w_gate, w_up), axis=1),
        preferred_element_type=jnp.float32,
    ).reshape(mixed.shape[:3] + (2 * hid,))
    fwd = both[:, 0].reshape(count, 2 * hid)
    bwd = both[:, 1].reshape(count, 2 * hid)
    hidden = (jax.nn.silu(fwd[:, :hid]) * fwd[:, hid:]).astype(jnp.bfloat16)
    d_hidden = lax.dot_general(
        grads, w_down, (((1,), (1,)), ((), ())), preferred_element_type=jnp.float32
    )
    a, b = bwd[:, :hid], bwd[:, hid:]
    sigm = 1.0 / (1.0 + jnp.exp(-a))
    d_first = (d_hidden * b * sigm * (1.0 + a * (1.0 - sigm))).astype(jnp.bfloat16)
    d_second = (d_hidden * a * sigm).astype(jnp.bfloat16)
    zero = jnp.zeros_like(hidden)
    left = jnp.concatenate(
        (
            jnp.concatenate((hidden, zero, zero), axis=1),
            jnp.concatenate((zero, d_first, d_second), axis=1),
        ),
        axis=0,
    )
    right = jnp.concatenate((w_down, w_gate.T, w_up.T), axis=0)
    return jnp.dot(left, right, preferred_element_type=jnp.float32).astype(jnp.bfloat16)


def body(
    fwd_tokens,
    fwd_routes,
    fwd_scores,
    bwd_tokens,
    bwd_routes,
    bwd_scores,
    out_grad,
    gate_weight,
    up_weight,
    down_weight,
):
    experts = lax.axis_size("eg")
    tokens = fwd_tokens.shape[1]
    topk = fwd_routes.shape[2]
    width = fwd_tokens.shape[2]
    capacity = min(tokens, max(6, (tokens * topk + experts - 1) // experts + 2))
    swap = [(0, 1), (1, 0)]
    own = (gate_weight[0], up_weight[0], down_weight[0])
    other = tuple(lax.ppermute(w, "c", swap) for w in own)
    w_gate = jnp.concatenate((own[0], other[0]), axis=1)
    w_up = jnp.concatenate((own[1], other[1]), axis=1)
    w_down = jnp.concatenate((own[2], other[2]), axis=0)
    member, weighted = route_tables(
        jnp.concatenate((fwd_routes, bwd_routes)),
        jnp.concatenate((fwd_scores, bwd_scores)),
        capacity,
        experts,
    )
    weight_f, member_b = weighted[0], member[1]
    pickers = jnp.stack((member[0], member_b, weighted[1]))
    sources = jnp.concatenate((fwd_tokens, bwd_tokens, out_grad)).astype(jnp.float32)
    chosen = jnp.einsum("kte,ktd->ked", pickers, sources, precision=lax.Precision.HIGHEST)
    lanes = 128
    payload = chosen.astype(jnp.bfloat16).reshape(3, experts, -1, lanes)
    crossed = lax.all_to_all(payload, "eg", split_axis=1, concat_axis=1, tiled=True)
    crossed = crossed.reshape(3, experts, capacity, width).transpose(0, 2, 1, 3)
    arrived = lax.all_gather(crossed, "p", axis=1, tiled=False)
    rows = arrived.reshape(3, -1, width)
    mixed = arrived.transpose(1, 2, 0, 3, 4).reshape(-1, 3, experts, width)
    parts = expert_pair(mixed, rows[2], w_gate, w_up, w_down)
    parts = parts.reshape(2, arrived.shape[1], -1, width)
    summed = lax.psum_scatter(parts, "p", scatter_dimension=1, tiled=True)
    summed = summed.reshape(2, capacity, experts, width).transpose(0, 2, 1, 3)
    summed = summed.reshape(2, experts, -1, lanes)
    home = lax.all_to_all(summed, "eg", split_axis=1, concat_axis=1, tiled=True)
    home = home.reshape(2, experts * capacity, width).astype(jnp.float32)
    layer_out = jnp.dot(weight_f, home[0], precision=lax.Precision.HIGHEST).astype(jnp.bfloat16)[
        None
    ]
    input_grad = jnp.dot(member_b, home[1], precision=lax.Precision.HIGHEST).astype(jnp.bfloat16)[
        None
    ]
    next_input = from_behind(layer_out, "pipe", 1)
    prev_grad = from_behind(input_grad, "pipe", -1)
    return (next_input, prev_grad)


def solution(mesh):
    pipe, expert = mesh.devices.shape
    shape = (pipe, expert // GROUP, GROUP // 2, 2)
    split = Mesh(mesh.devices.reshape(shape), ("pipe", "eg", "p", "c"))
    rows = P("pipe", ("eg", "p", "c"), None)
    cols = P("pipe", None, ("eg", "p", "c"))
    placed = (rows, rows, rows, rows, rows, rows, rows, cols, cols, rows)
    return jax.shard_map(
        body,
        mesh=split,
        in_specs=placed,
        out_specs=(rows, rows),
        check_vma=False,
    )
```

```python
import jax
import jax.numpy as jnp
from jax import lax
from jax.sharding import Mesh
from jax.sharding import PartitionSpec as P

GROUP = 8


def from_behind(value, axis, steps):
    count = lax.axis_size(axis)
    pairs = [(source, (source + steps) % count) for source in range(count)]
    return lax.ppermute(value, axis, pairs)


def route_tables(routes, scores, capacity, experts):
    kinds, tokens, topk = routes.shape
    flat = routes.reshape(kinds, -1)
    onehot = (flat[:, :, None] == jnp.arange(experts, dtype=jnp.int32)).astype(jnp.int32)
    rank = jnp.cumsum(onehot, axis=1) - onehot
    within = jnp.sum(rank * onehot, axis=2)
    slot_ids = (flat * capacity + within).reshape(kinds, tokens, topk)
    places = jnp.arange(experts * capacity, dtype=jnp.int32)
    hits = (slot_ids[..., None] == places).astype(jnp.float32)
    normed = scores / jnp.sum(scores, axis=2, keepdims=True)
    member = jnp.sum(hits, axis=2)
    weighted = jnp.sum(hits * normed[..., None], axis=2)
    return (member, weighted)


def pick_rows(member, rows):
    slots = jnp.einsum(
        "te,td->ed", member.astype(jnp.bfloat16), rows, preferred_element_type=jnp.float32
    )
    return slots.astype(jnp.bfloat16)


def expert_pair(rows, grads, w_gate, w_up, w_down):
    count = grads.shape[0]
    hid = w_gate.shape[1]
    both = jnp.dot(rows, jnp.concatenate((w_gate, w_up), axis=1), preferred_element_type=jnp.float32)
    first, second = both[:, :hid], both[:, hid:]
    hidden = (jax.nn.silu(first[:count]) * second[:count]).astype(jnp.bfloat16)
    d_hidden = lax.dot_general(
        grads, w_down, (((1,), (1,)), ((), ())), preferred_element_type=jnp.float32
    )
    a, b = first[count:], second[count:]
    sigm = 1.0 / (1.0 + jnp.exp(-a))
    d_first = (d_hidden * b * sigm * (1.0 + a * (1.0 - sigm))).astype(jnp.bfloat16)
    d_second = (d_hidden * a * sigm).astype(jnp.bfloat16)
    zero = jnp.zeros_like(hidden)
    left = jnp.concatenate(
        (
            jnp.concatenate((hidden, zero, zero), axis=1),
            jnp.concatenate((zero, d_first, d_second), axis=1),
        ),
        axis=0,
    )
    right = jnp.concatenate((w_down, w_gate.T, w_up.T), axis=0)
    chips = lax.axis_size("p")
    left = left.reshape(2, chips, -1, left.shape[-1]).transpose(1, 0, 2, 3).reshape(left.shape)
    out = jnp.dot(left, right, preferred_element_type=jnp.float32).astype(jnp.bfloat16)
    return out.reshape(chips, 2, -1, out.shape[-1]).transpose(1, 0, 2, 3).reshape(out.shape)


def body(
    fwd_tokens,
    fwd_routes,
    fwd_scores,
    bwd_tokens,
    bwd_routes,
    bwd_scores,
    out_grad,
    gate_weight,
    up_weight,
    down_weight,
):
    experts = lax.axis_size("eg")
    tokens = fwd_tokens.shape[1]
    topk = fwd_routes.shape[2]
    width = fwd_tokens.shape[2]
    capacity = min(tokens, max(6, (tokens * topk + experts - 1) // experts + 2))
    swap = [(0, 1), (1, 0)]
    own = (gate_weight[0], up_weight[0], down_weight[0])
    other = tuple(lax.ppermute(w, "c", swap) for w in own)
    w_gate = jnp.concatenate((own[0], other[0]), axis=1)
    w_up = jnp.concatenate((own[1], other[1]), axis=1)
    w_down = jnp.concatenate((own[2], other[2]), axis=0)
    member, weighted = route_tables(
        jnp.concatenate((fwd_routes, bwd_routes)),
        jnp.concatenate((fwd_scores, bwd_scores)),
        capacity,
        experts,
    )
    weight_f, member_b = weighted[0], member[1]
    pickers = jnp.stack((member[0], member_b, weighted[1]))
    sources = jnp.concatenate((fwd_tokens, bwd_tokens, out_grad)).astype(jnp.float32)
    chosen = jnp.einsum("kte,ktd->ked", pickers, sources, precision=lax.Precision.HIGHEST)
    lanes = 128
    payload = chosen.astype(jnp.bfloat16).reshape(3, experts, -1, lanes)
    crossed = lax.all_to_all(payload, "eg", split_axis=1, concat_axis=1, tiled=True)
    crossed = crossed.reshape(3, experts, capacity, width).transpose(0, 2, 1, 3)
    arrived = lax.all_gather(crossed, "p", axis=1, tiled=False)
    rows = arrived.reshape(3, -1, width)
    parts = expert_pair(rows[:2].reshape(-1, width), rows[2], w_gate, w_up, w_down)
    parts = parts.reshape(2, arrived.shape[1], -1, width)
    summed = lax.psum_scatter(parts, "p", scatter_dimension=1, tiled=True)
    summed = summed.reshape(2, capacity, experts, width).transpose(0, 2, 1, 3)
    summed = summed.reshape(2, experts, -1, lanes)
    home = lax.all_to_all(summed, "eg", split_axis=1, concat_axis=1, tiled=True)
    home = home.reshape(2, experts * capacity, width).astype(jnp.float32)
    layer_out = jnp.dot(weight_f, home[0], precision=lax.Precision.HIGHEST).astype(jnp.bfloat16)[
        None
    ]
    input_grad = jnp.dot(member_b, home[1], precision=lax.Precision.HIGHEST).astype(jnp.bfloat16)[
        None
    ]
    next_input = from_behind(layer_out, "pipe", 1)
    prev_grad = from_behind(input_grad, "pipe", -1)
    return (next_input, prev_grad)


def solution(mesh):
    pipe, expert = mesh.devices.shape
    shape = (pipe, expert // GROUP, GROUP // 2, 2)
    split = Mesh(mesh.devices.reshape(shape), ("pipe", "eg", "p", "c"))
    rows = P("pipe", ("eg", "p", "c"), None)
    cols = P("pipe", None, ("eg", "p", "c"))
    placed = (rows, rows, rows, rows, rows, rows, rows, cols, cols, rows)
    return jax.shard_map(
        body,
        mesh=split,
        in_specs=placed,
        out_specs=(rows, rows),
        check_vma=False,
    )
```
